32 devices in a mesh: row: 4 (over z), col: 4 (over y, x), batch: 2 (over core).
Axes of the slice: x: 2, y: 2, z: 4, core: 2. Of those that a mesh axis runs over, the one named last changes fastest.
Arguments:
- green: bfloat16 [4, 4, 2048, 2048], P('row', 'col'), may hold values from -0.125 to 0.125
- background: bfloat16 [4, 4, 512, 2048], P('row', 'col', 'batch'), parts along dimension 2, may hold values from -3 to 3
- wavelet: bfloat16 [512, 2048], P('batch'), parts along dimension 0, may hold values from -6 to 6
- station_cell: int32 [512], P('batch'), parts along dimension 0, may hold values from 0 to 15
- fault_point: int32 [4, 64], P('row', 'col'), may hold values from 0 to 2047
- fault_owner: int32 [4, 64, 1], P('row', 'col'), may hold values from 0 to 3; in each aligned block of 16 rows (0 to 15, 16 to 31, ..., all dimensions but the last counted through in order) at most 8 rows name the same one
- fault_row: int32 [4, 64], P('row', 'col'), may hold values from 0 to 127
Outputs:
- sweep: bfloat16 [4, 4, 512, 2048], P('row', 'col', 'batch'), parts along dimension 2
- database: float32 [4, 4, 128, 512], P('row', 'col', None, 'batch'), parts along dimension 3
The draws below stay inside these ranges and needn't reach their ends.
There are 2 independent parts, one for each index of `batch`. The reference program is written for one: setup_inputs(seed, part) draws one part's arguments, and reference() takes and returns one part's arrays. A program takes and returns all parts, laid end to end along the dimension named above; an argument that names none is the same for every part. Nothing has to cross between parts.
Inputs may be any that keep to these rules, and one draw needn't show every extreme that they name: `fault_owner`: among the 16 fault points of one subdomain no owner is named more than 8 times, and in every draw some subdomain names some owner exactly 8 times.
All inputs are finite; a program needn't handle non-finite values.
Results may differ from the reference program's by a relative error of at most 0.02.
Values may be sent and summed in bfloat16 or wider, within the bound.
No kernel may reach another device: no remote copies, remote signals or barrier semaphores. Data moves between devices by JAX's collectives and lax.ppermute only.
A program may use at most 64 MiB of HBM per device.

```python
import math
import jax
import jax.numpy as jnp
import numpy as np

F = 1024
S = 256
DB = 128
Q = 16
CAP = 8
CELLS = 16
N_ROW = 4
N_COL = 4


def set_ends(entries, key, smallest, high):
    longest = entries.shape.index(max(entries.shape))
    spots = []
    for shift in (0, 1):
        where = [jax.random.randint(jax.random.fold_in(key, axis), (), 0, length) for axis, length in enumerate(entries.shape)]
        where[longest] = (where[longest] + shift) % entries.shape[longest]
        spots.append(tuple(where))
    return entries.at[spots[0]].set(smallest).at[spots[1]].set(high)


def shard_levels(own_key, dims, pieces, low, top_value):
    level = 1.0
    for axis_at, blocks in pieces:
        steps = jax.random.uniform(jax.random.fold_in(jax.random.fold_in(own_key, 6), axis_at), (blocks,), jnp.float32, low / len(pieces), top_value / len(pieces))
        level = level * jnp.repeat(jnp.exp(steps), dims[axis_at] // blocks).reshape((-1,) + (1,) * (len(dims) - 1 - axis_at))
    return level


def shared_out(stream_key, own, number, rows, count, top, limit, slope):
    order = jax.random.permutation(stream_key, count)
    heavy_load, common = portions_of(count, rows * top, limit, slope, True), portions_of(count, rows * top, limit, slope, False)
    places = jnp.arange(count)

    def named(tallies, rotation):
        used = int((tallies > 0).sum())
        fixed = max(1, used // 4)
        shifted = fixed + (places - fixed + rotation * (used - fixed)) % max(1, count - fixed)
        return jnp.zeros((count,), jnp.int32).at[order[jnp.where(places < fixed, places, shifted)]].set(jnp.asarray(tallies, jnp.int32))

    tallies = jnp.where(number % 4 == 0, named(heavy_load, number // 4), named(common, number - number // 4 - 1))
    mixed = jax.random.permutation(jax.random.fold_in(own, 3), count)
    giver, receiver = mixed[0:count // 2 * 2:2], mixed[1:count // 2 * 2:2]
    room = jnp.minimum(tallies[giver] - 1, limit - tallies[receiver]) // 2
    room = jnp.where((giver == order[0]) | (receiver == order[0]) | (tallies[receiver] == 0), 0, jnp.maximum(room, 0))
    shifted = jax.random.randint(jax.random.fold_in(own, 4), (count // 2,), 0, 1 << 20) % (room + 1)
    tallies = tallies.at[giver].add(-shifted).at[receiver].add(shifted)
    items = jnp.searchsorted(jnp.cumsum(tallies), jnp.arange(rows * top), side="right").astype(jnp.int32)
    listing = items.reshape(top, rows).T
    listing = listing[jax.random.permutation(jax.random.fold_in(own, 1), rows)]
    rotation = jax.random.randint(jax.random.fold_in(own, 2), (rows, 1), 0, top)
    return jnp.take_along_axis(listing, (jnp.arange(top)[None, :] + rotation) % top, axis=1)


def portions_of(count, total, most, lean, full):
    portions = [(1 << 20) // math.isqrt(standing ** lean) + 1 for standing in range(1, count + 1)]
    largest = most if full else min(most, max(-(-total // count), total * portions[0] // sum(portions)))
    least = 1 if total - largest >= count - 1 else 0
    holding, spare = [largest] + [least] * (count - 1), total - largest - least * (count - 1)
    while spare > 0:
        candidates = [i for i in range(1, count) if holding[i] < largest] or [i for i in range(1, count) if holding[i] < most]
        pool, remaining = sum([portions[i] for i in candidates]), spare
        for i in candidates:
            addition = min(most - holding[i], max(1, remaining * portions[i] // pool), spare)
            holding[i] = holding[i] + addition
            spare = spare - addition
    return np.array(holding)


def gaussian(own_key, shape, spread, most, shards=(), kind=jnp.bfloat16):
    level = shard_levels(own_key, shape, shards, -0.22, 0.18) if shards else 1.0
    drawn = jax.random.normal(own_key, shape, jnp.float32) * spread * level
    return jnp.minimum(jnp.maximum(drawn, -most), most).astype(kind)


def setup_inputs(seed: int = 0, part: int = 0) -> dict:
    key_of = jax.random.split(jax.random.key(seed), 8)
    part_splits = jax.random.split(jax.random.fold_in(key_of[7], part), 8)
    green = gaussian(key_of[0], (N_ROW, N_COL, 2 * F, 2 * F), (2 * F) ** -0.5, 0.125, ((0, 4), (1, 4)))
    background = gaussian(part_splits[1], (N_ROW, N_COL, S, 2 * F), 0.5, 3.0, ((0, 4), (1, 4)))
    wavelet = gaussian(part_splits[2], (S, 2 * F), 1.0, 6.0)
    station_cell = set_ends(jax.random.randint(part_splits[3], (S,), 0, CELLS), jax.random.fold_in(part_splits[3], 1), 0, CELLS - 1).astype(jnp.int32)
    fault_point = set_ends(jax.random.randint(key_of[4], (N_ROW, N_COL * Q), 0, 2 * F), jax.random.fold_in(key_of[4], 1), 0, (2 * F) - 1).astype(jnp.int32)
    fault_owner_keys = jax.random.split(jax.random.fold_in(key_of[5], 1), N_ROW * (N_COL * Q) // Q)
    fault_owner_turns = jax.random.permutation(jax.random.fold_in(key_of[5], 3), N_ROW * (N_COL * Q) // Q)
    fault_owner = jax.vmap(lambda own, number: shared_out(jax.random.fold_in(key_of[5], 2), own, number, Q, N_COL, 1, CAP, 2))(fault_owner_keys, fault_owner_turns).reshape((N_ROW, N_COL * Q, 1))
    fault_row = set_ends(jax.random.randint(key_of[6], (N_ROW, N_COL * Q), 0, DB), jax.random.fold_in(key_of[6], 1), 0, DB - 1).astype(jnp.int32)
    return {"green": green, "background": background, "wavelet": wavelet, "station_cell": station_cell, "fault_point": fault_point, "fault_owner": fault_owner, "fault_row": fault_row}


def reference(green, background, wavelet, station_cell, fault_point, fault_owner, fault_row):
    rows_total = green.shape[0]
    cols_total = green.shape[1]
    half = green.shape[2] // 2
    stations = background.shape[2]
    listed = fault_point.shape[1] // cols_total
    wave_float = wavelet.astype(jnp.float32)
    results = [[None] * cols_total for _ in range(rows_total)]
    for row_place in range(rows_total):
        for col_place in range(cols_total):
            if row_place > 0:
                down_in = results[row_place - 1][col_place][:, :half]
            else:
                down_in = jnp.zeros((stations, half), jnp.bfloat16)
            if col_place > 0:
                right_in = results[row_place][col_place - 1][:, half:]
            else:
                right_in = jnp.zeros((stations, half), jnp.bfloat16)
            joined = jnp.concatenate([down_in, right_in], axis=1)
            own = (station_cell == row_place * cols_total + col_place)[:, None]
            source = background[row_place, col_place].astype(jnp.float32) + jnp.where(own, wave_float, jnp.zeros_like(wave_float))
            update = jnp.dot(joined, green[row_place, col_place], preferred_element_type=jnp.float32) + source
            results[row_place][col_place] = update.astype(jnp.bfloat16)
    sweep = jnp.stack([jnp.stack(line, axis=0) for line in results], axis=0)
    tables = []
    for row_place in range(rows_total):
        total = jnp.zeros((cols_total * DB, stations), jnp.float32)
        for col_place in range(cols_total):
            points = fault_point[row_place, col_place * listed:(col_place + 1) * listed]
            owners = fault_owner[row_place, col_place * listed:(col_place + 1) * listed, 0]
            targets = fault_row[row_place, col_place * listed:(col_place + 1) * listed]
            traces = results[row_place][col_place][:, points].astype(jnp.float32).T
            keys = (owners * DB + targets).astype(jnp.int32)
            total = total + jax.ops.segment_sum(traces, keys, num_segments=cols_total * DB)
        tables.append(total.reshape(cols_total, DB, stations))
    database = jnp.stack(tables, axis=0)
    return sweep, database
```

```python
import jax
import jax.numpy as jnp
from jax import lax
from jax.sharding import PartitionSpec as P

DB = 128
BLOCKS = 2
ORDER = 'rl'


def passed_along(shard, axis, by):
    peers = lax.axis_size(axis)
    pairs = [(i, i + by) for i in range(peers) if 0 <= i + by < peers]
    return lax.ppermute(shard, axis, pairs)


def on_device(green, background, wavelet, station_cell, fault_point, fault_owner, fault_row):
    row_place = lax.axis_index("row")
    col_place = lax.axis_index("col")
    row_count = lax.axis_size("row")
    col_count = lax.axis_size("col")
    matrix = green[0, 0]
    half = matrix.shape[0] // 2
    stations = background.shape[2]
    own_source = (station_cell == row_place * col_count + col_place)[:, None]
    source = background[0, 0].astype(jnp.float32) + jnp.where(
        own_source, wavelet.astype(jnp.float32), 0.0
    )
    height = stations // BLOCKS
    total_fronts = row_count + col_count + BLOCKS - 2
    down_in = jnp.zeros((height, half), jnp.bfloat16)
    right_in = jnp.zeros((height, half), jnp.bfloat16)
    field = jnp.zeros((stations, 2 * half), jnp.bfloat16)
    for moment in range(total_fronts):
        block = moment - row_place - col_place
        active = jnp.logical_and(block >= 0, block < BLOCKS)
        start = jnp.clip(block, 0, BLOCKS - 1) * height
        part = lax.dynamic_slice_in_dim(source, start, height, 0)
        joined = jnp.concatenate([down_in, right_in], axis=1)
        if ORDER == "one":
            update = (jnp.dot(joined, matrix, preferred_element_type=jnp.float32) + part).astype(jnp.bfloat16)
            lower, right = update[:, :half], update[:, half:]
            right_next = passed_along(right, "col", 1)
            down_next = passed_along(lower, "row", 1)
        else:
            def face(lo):
                cols = slice(0, half) if lo else slice(half, 2 * half)
                return (jnp.dot(joined, matrix[:, cols], preferred_element_type=jnp.float32) + part[:, cols]).astype(jnp.bfloat16)
            if ORDER == "rl":
                right = face(False)
                right_next = passed_along(right, "col", 1)
                lower = face(True)
                down_next = passed_along(lower, "row", 1)
            else:
                lower = face(True)
                down_next = passed_along(lower, "row", 1)
                right = face(False)
                right_next = passed_along(right, "col", 1)
            update = jnp.concatenate([lower, right], axis=1)
        previous = lax.dynamic_slice_in_dim(field, start, height, 0)
        field = lax.dynamic_update_slice_in_dim(field, jnp.where(active, update, previous), start, 0)
        down_in, right_in = down_next, right_next
    points = fault_point[0]
    owners = fault_owner[0, :, 0]
    targets = fault_row[0]
    listed = points.shape[0]
    point_hot = (points[:, None] == jnp.arange(2 * half, dtype=jnp.int32)[None, :]).astype(jnp.bfloat16)
    traces = jnp.einsum("qp,sp->qs", point_hot, field, preferred_element_type=jnp.float32).astype(jnp.bfloat16)
    capacity = 2 * listed // col_count
    owner_hot = (owners[:, None] == jnp.arange(col_count, dtype=jnp.int32)[None, :]).astype(jnp.int32)
    running = jnp.cumsum(owner_hot, axis=0) - 1
    rank = jnp.sum(owner_hot * running, axis=1)
    slots = owners * capacity + rank
    slot_match = slots[None, :] == jnp.arange(col_count * capacity, dtype=jnp.int32)[:, None]
    slot_hot = slot_match.astype(jnp.bfloat16)
    packed = jnp.dot(slot_hot, traces, preferred_element_type=jnp.float32).astype(jnp.bfloat16)
    slot_rows = jnp.sum(jnp.where(slot_match, targets[None, :] + 1, 0), axis=1) - 1
    tag = jnp.broadcast_to(slot_rows.astype(jnp.bfloat16)[:, None], (col_count * capacity, 128))
    message = jnp.concatenate([packed, tag], axis=1).reshape(col_count, capacity, stations + 128)
    arrived = lax.all_to_all(message, "col", split_axis=0, concat_axis=0, tiled=True)
    arrived = arrived.reshape(col_count * capacity, stations + 128)
    row_numbers = arrived[:, stations].astype(jnp.int32)
    table_hot = (row_numbers[None, :] == jnp.arange(DB, dtype=jnp.int32)[:, None]).astype(jnp.bfloat16)
    database = jnp.dot(table_hot, arrived[:, :stations], preferred_element_type=jnp.float32)
    return (field[None, None], database[None, None])


def solution(mesh):
    in_specs = (
        P("row", "col", None, None),
        P("row", "col", "batch", None),
        P("batch", None),
        P("batch"),
        P("row", "col"),
        P("row", "col", None),
        P("row", "col"),
    )
    out_specs = (P("row", "col", "batch", None), P("row", "col", None, "batch"))
    return jax.shard_map(
        on_device, mesh=mesh, in_specs=in_specs, out_specs=out_specs, check_vma=False
    )
```

```python
import jax
import jax.numpy as jnp
from jax import lax
from jax.sharding import PartitionSpec as P

DB = 128
BLOCKS = 2
SKEW = 1


def passed_along(shard, moment, down, rows, cols):
    pairs = []
    for r in range(rows):
        for c in range(cols):
            if not 0 <= moment - SKEW * (r + c) < BLOCKS:
                continue
            if down and r + 1 < rows:
                pairs.append((r * cols + c, (r + 1) * cols + c))
            if not down and c + 1 < cols:
                pairs.append((r * cols + c, r * cols + c + 1))
    if not pairs:
        return jnp.zeros_like(shard)
    return lax.ppermute(shard, ("row", "col"), pairs)


def on_device(green, background, wavelet, station_cell, fault_point, fault_owner, fault_row):
    row_place = lax.axis_index("row")
    col_place = lax.axis_index("col")
    row_count = lax.axis_size("row")
    col_count = lax.axis_size("col")
    matrix = green[0, 0]
    half = matrix.shape[0] // 2
    stations = background.shape[2]
    own_source = (station_cell == row_place * col_count + col_place)[:, None]
    source = background[0, 0].astype(jnp.float32) + jnp.where(
        own_source, wavelet.astype(jnp.float32), 0.0
    )
    height = stations // BLOCKS
    total_fronts = SKEW * (row_count + col_count - 2) + BLOCKS
    down_in = jnp.zeros((height, half), jnp.bfloat16)
    right_in = jnp.zeros((height, half), jnp.bfloat16)
    field = jnp.zeros((stations, 2 * half), jnp.bfloat16)
    inbox = {}
    for moment in range(total_fronts):
        block = moment - SKEW * (row_place + col_place)
        active = jnp.logical_and(block >= 0, block < BLOCKS)
        start = jnp.clip(block, 0, BLOCKS - 1) * height
        part = lax.dynamic_slice_in_dim(source, start, height, 0)
        if moment < SKEW:
            lower = part[:, :half].astype(jnp.bfloat16)
            right = part[:, half:].astype(jnp.bfloat16)
        else:
            down_in, right_in = inbox.pop(moment)
            joined = jnp.concatenate([down_in, right_in], axis=1)
            right = (jnp.dot(joined, matrix[:, half:], preferred_element_type=jnp.float32) + part[:, half:]).astype(jnp.bfloat16)
            lower = (jnp.dot(joined, matrix[:, :half], preferred_element_type=jnp.float32) + part[:, :half]).astype(jnp.bfloat16)
        right_next = passed_along(right, moment, False, row_count, col_count)
        down_next = passed_along(lower, moment, True, row_count, col_count)
        inbox[moment + SKEW] = (down_next, right_next)
        update = jnp.concatenate([lower, right], axis=1)
        previous = lax.dynamic_slice_in_dim(field, start, height, 0)
        field = lax.dynamic_update_slice_in_dim(field, jnp.where(active, update, previous), start, 0)
    points = fault_point[0]
    owners = fault_owner[0, :, 0]
    targets = fault_row[0]
    listed = points.shape[0]
    point_hot = (points[:, None] == jnp.arange(2 * half, dtype=jnp.int32)[None, :]).astype(jnp.bfloat16)
    traces = jnp.einsum("qp,sp->qs", point_hot, field, preferred_element_type=jnp.float32).astype(jnp.bfloat16)
    capacity = 2 * listed // col_count
    owner_hot = (owners[:, None] == jnp.arange(col_count, dtype=jnp.int32)[None, :]).astype(jnp.int32)
    running = jnp.cumsum(owner_hot, axis=0) - 1
    rank = jnp.sum(owner_hot * running, axis=1)
    slots = owners * capacity + rank
    slot_match = slots[None, :] == jnp.arange(col_count * capacity, dtype=jnp.int32)[:, None]
    slot_hot = slot_match.astype(jnp.bfloat16)
    packed = jnp.dot(slot_hot, traces, preferred_element_type=jnp.float32).astype(jnp.bfloat16)
    slot_rows = jnp.sum(jnp.where(slot_match, targets[None, :] + 1, 0), axis=1) - 1
    tag = jnp.broadcast_to(slot_rows.astype(jnp.bfloat16)[:, None], (col_count * capacity, 128))
    message = jnp.concatenate([packed, tag], axis=1).reshape(col_count, capacity, stations + 128)
    arrived = lax.all_to_all(message, "col", split_axis=0, concat_axis=0, tiled=True)
    arrived = arrived.reshape(col_count * capacity, stations + 128)
    row_numbers = arrived[:, stations].astype(jnp.int32)
    table_hot = (row_numbers[None, :] == jnp.arange(DB, dtype=jnp.int32)[:, None]).astype(jnp.bfloat16)
    database = jnp.dot(table_hot, arrived[:, :stations], preferred_element_type=jnp.float32)
    return (field[None, None], database[None, None])


def solution(mesh):
    in_specs = (
        P("row", "col", None, None),
        P("row", "col", "batch", None),
        P("batch", None),
        P("batch"),
        P("row", "col"),
        P("row", "col", None),
        P("row", "col"),
    )
    out_specs = (P("row", "col", "batch", None), P("row", "col", None, "batch"))
    return jax.shard_map(
        on_device, mesh=mesh, in_specs=in_specs, out_specs=out_specs, check_vma=False
    )
```

```python
import jax
import jax.numpy as jnp
from jax import lax
from jax.sharding import PartitionSpec as P

DB = 128
BLOCKS = 2
SKEW = 1


def passed_along(shard, moment, down, rows, cols):
    pairs = []
    for r in range(rows):
        for c in range(cols):
            if not 0 <= moment - SKEW * (r + c) < BLOCKS:
                continue
            if down and r + 1 < rows:
                pairs.append((r * cols + c, (r + 1) * cols + c))
            if not down and c + 1 < cols:
                pairs.append((r * cols + c, r * cols + c + 1))
    if not pairs:
        return jnp.zeros_like(shard)
    return lax.ppermute(shard, ("row", "col"), pairs)


def on_device(green, background, wavelet, station_cell, fault_point, fault_owner, fault_row):
    row_place = lax.axis_index("row")
    col_place = lax.axis_index("col")
    row_count = lax.axis_size("row")
    col_count = lax.axis_size("col")
    matrix = green[0, 0]
    half = matrix.shape[0] // 2
    stations = background.shape[2]
    own_source = (station_cell == row_place * col_count + col_place)[:, None]
    source = background[0, 0].astype(jnp.float32) + jnp.where(
        own_source, wavelet.astype(jnp.float32), 0.0
    )
    height = stations // BLOCKS
    total_fronts = SKEW * (row_count + col_count - 2) + BLOCKS
    down_in = jnp.zeros((height, half), jnp.bfloat16)
    right_in = jnp.zeros((height, half), jnp.bfloat16)
    field = jnp.zeros((stations, 2 * half), jnp.bfloat16)
    inbox = {}
    for moment in range(total_fronts):
        block = moment - SKEW * (row_place + col_place)
        active = jnp.logical_and(block >= 0, block < BLOCKS)
        start = jnp.clip(block, 0, BLOCKS - 1) * height
        part = lax.dynamic_slice_in_dim(source, start, height, 0)
        if moment < SKEW:
            lower = part[:, :half].astype(jnp.bfloat16)
            right = part[:, half:].astype(jnp.bfloat16)
        elif moment == SKEW and SKEW == 1:
            down_in, right_in = inbox.pop(moment)
            arrived = down_in + right_in
            rows_from = jnp.where(row_place == 0, half, 0)
            rows = lax.dynamic_slice_in_dim(matrix, rows_from, half, 0)
            right = (jnp.dot(arrived, rows[:, half:], preferred_element_type=jnp.float32) + part[:, half:]).astype(jnp.bfloat16)
            lower = (jnp.dot(arrived, rows[:, :half], preferred_element_type=jnp.float32) + part[:, :half]).astype(jnp.bfloat16)
        else:
            down_in, right_in = inbox.pop(moment)
            joined = jnp.concatenate([down_in, right_in], axis=1)
            right = (jnp.dot(joined, matrix[:, half:], preferred_element_type=jnp.float32) + part[:, half:]).astype(jnp.bfloat16)
            lower = (jnp.dot(joined, matrix[:, :half], preferred_element_type=jnp.float32) + part[:, :half]).astype(jnp.bfloat16)
        right_next = passed_along(right, moment, False, row_count, col_count)
        down_next = passed_along(lower, moment, True, row_count, col_count)
        inbox[moment + SKEW] = (down_next, right_next)
        update = jnp.concatenate([lower, right], axis=1)
        previous = lax.dynamic_slice_in_dim(field, start, height, 0)
        field = lax.dynamic_update_slice_in_dim(field, jnp.where(active, update, previous), start, 0)
    points = fault_point[0]
    owners = fault_owner[0, :, 0]
    targets = fault_row[0]
    listed = points.shape[0]
    point_hot = (points[:, None] == jnp.arange(2 * half, dtype=jnp.int32)[None, :]).astype(jnp.bfloat16)
    traces = jnp.einsum("qp,sp->qs", point_hot, field, preferred_element_type=jnp.float32).astype(jnp.bfloat16)
    capacity = 2 * listed // col_count
    owner_hot = (owners[:, None] == jnp.arange(col_count, dtype=jnp.int32)[None, :]).astype(jnp.int32)
    running = jnp.cumsum(owner_hot, axis=0) - 1
    rank = jnp.sum(owner_hot * running, axis=1)
    slots = owners * capacity + rank
    slot_match = slots[None, :] == jnp.arange(col_count * capacity, dtype=jnp.int32)[:, None]
    slot_hot = slot_match.astype(jnp.bfloat16)
    packed = jnp.dot(slot_hot, traces, preferred_element_type=jnp.float32).astype(jnp.bfloat16)
    slot_rows = jnp.sum(jnp.where(slot_match, targets[None, :] + 1, 0), axis=1) - 1
    tag = jnp.broadcast_to(slot_rows.astype(jnp.bfloat16)[:, None], (col_count * capacity, 128))
    message = jnp.concatenate([packed, tag], axis=1).reshape(col_count, capacity, stations + 128)
    arrived = lax.all_to_all(message, "col", split_axis=0, concat_axis=0, tiled=True)
    arrived = arrived.reshape(col_count * capacity, stations + 128)
    row_numbers = arrived[:, stations].astype(jnp.int32)
    table_hot = (row_numbers[None, :] == jnp.arange(DB, dtype=jnp.int32)[:, None]).astype(jnp.bfloat16)
    database = jnp.dot(table_hot, arrived[:, :stations], preferred_element_type=jnp.float32)
    return (field[None, None], database[None, None])


def solution(mesh):
    in_specs = (
        P("row", "col", None, None),
        P("row", "col", "batch", None),
        P("batch", None),
        P("batch"),
        P("row", "col"),
        P("row", "col", None),
        P("row", "col"),
    )
    out_specs = (P("row", "col", "batch", None), P("row", "col", None, "batch"))
    return jax.shard_map(
        on_device, mesh=mesh, in_specs=in_specs, out_specs=out_specs, check_vma=False
    )
```

```python
import jax
import jax.numpy as jnp
from jax import lax
from jax.sharding import PartitionSpec as P

DB = 128
BLOCKS = 2
SKEW = 1


def passed_along(shard, moment, down, rows, cols):
    pairs = []
    for r in range(rows):
        for c in range(cols):
            if not 0 <= moment - SKEW * (r + c) < BLOCKS:
                continue
            if down and r + 1 < rows:
                pairs.append((r * cols + c, (r + 1) * cols + c))
            if not down and c + 1 < cols:
                pairs.append((r * cols + c, r * cols + c + 1))
    if not pairs:
        return jnp.zeros_like(shard)
    return lax.ppermute(shard, ("row", "col"), pairs)


def on_device(green, background, wavelet, station_cell, fault_point, fault_owner, fault_row):
    row_place = lax.axis_index("row")
    col_place = lax.axis_index("col")
    row_count = lax.axis_size("row")
    col_count = lax.axis_size("col")
    matrix = green[0, 0]
    half = matrix.shape[0] // 2
    to_right, to_lower = lax.optimization_barrier((matrix[:, half:], matrix[:, :half]))
    stations = background.shape[2]
    own_source = (station_cell == row_place * col_count + col_place)[:, None]
    source = background[0, 0].astype(jnp.float32) + jnp.where(
        own_source, wavelet.astype(jnp.float32), 0.0
    )
    height = stations // BLOCKS
    total_fronts = SKEW * (row_count + col_count - 2) + BLOCKS
    down_in = jnp.zeros((height, half), jnp.bfloat16)
    right_in = jnp.zeros((height, half), jnp.bfloat16)
    field = jnp.zeros((stations, 2 * half), jnp.bfloat16)
    inbox = {}
    for moment in range(total_fronts):
        block = moment - SKEW * (row_place + col_place)
        active = jnp.logical_and(block >= 0, block < BLOCKS)
        start = jnp.clip(block, 0, BLOCKS - 1) * height
        part = lax.dynamic_slice_in_dim(source, start, height, 0)
        if moment < SKEW:
            lower = part[:, :half].astype(jnp.bfloat16)
            right = part[:, half:].astype(jnp.bfloat16)
        elif moment == SKEW and SKEW == 1:
            down_in, right_in = inbox.pop(moment)
            arrived = down_in + right_in
            rows_from = jnp.where(row_place == 0, half, 0)
            right_rows = lax.dynamic_slice_in_dim(to_right, rows_from, half, 0)
            lower_rows = lax.dynamic_slice_in_dim(to_lower, rows_from, half, 0)
            right = (jnp.dot(arrived, right_rows, preferred_element_type=jnp.float32) + part[:, half:]).astype(jnp.bfloat16)
            lower = (jnp.dot(arrived, lower_rows, preferred_element_type=jnp.float32) + part[:, :half]).astype(jnp.bfloat16)
        else:
            down_in, right_in = inbox.pop(moment)
            joined = jnp.concatenate([down_in, right_in], axis=1)
            right = (jnp.dot(joined, to_right, preferred_element_type=jnp.float32) + part[:, half:]).astype(jnp.bfloat16)
            lower = (jnp.dot(joined, to_lower, preferred_element_type=jnp.float32) + part[:, :half]).astype(jnp.bfloat16)
        right_next = passed_along(right, moment, False, row_count, col_count)
        down_next = passed_along(lower, moment, True, row_count, col_count)
        inbox[moment + SKEW] = (down_next, right_next)
        update = jnp.concatenate([lower, right], axis=1)
        previous = lax.dynamic_slice_in_dim(field, start, height, 0)
        field = lax.dynamic_update_slice_in_dim(field, jnp.where(active, update, previous), start, 0)
    points = fault_point[0]
    owners = fault_owner[0, :, 0]
    targets = fault_row[0]
    listed = points.shape[0]
    point_hot = (points[:, None] == jnp.arange(2 * half, dtype=jnp.int32)[None, :]).astype(jnp.bfloat16)
    traces = jnp.einsum("qp,sp->qs", point_hot, field, preferred_element_type=jnp.float32).astype(jnp.bfloat16)
    capacity = 2 * listed // col_count
    owner_hot = (owners[:, None] == jnp.arange(col_count, dtype=jnp.int32)[None, :]).astype(jnp.int32)
    running = jnp.cumsum(owner_hot, axis=0) - 1
    rank = jnp.sum(owner_hot * running, axis=1)
    slots = owners * capacity + rank
    slot_match = slots[None, :] == jnp.arange(col_count * capacity, dtype=jnp.int32)[:, None]
    slot_hot = slot_match.astype(jnp.bfloat16)
    packed = jnp.dot(slot_hot, traces, preferred_element_type=jnp.float32).astype(jnp.bfloat16)
    slot_rows = jnp.sum(jnp.where(slot_match, targets[None, :] + 1, 0), axis=1) - 1
    tag = jnp.broadcast_to(slot_rows.astype(jnp.bfloat16)[:, None], (col_count * capacity, 128))
    message = jnp.concatenate([packed, tag], axis=1).reshape(col_count, capacity, stations + 128)
    arrived = lax.all_to_all(message, "col", split_axis=0, concat_axis=0, tiled=True)
    arrived = arrived.reshape(col_count * capacity, stations + 128)
    row_numbers = arrived[:, stations].astype(jnp.int32)
    table_hot = (row_numbers[None, :] == jnp.arange(DB, dtype=jnp.int32)[:, None]).astype(jnp.bfloat16)
    database = jnp.dot(table_hot, arrived[:, :stations], preferred_element_type=jnp.float32)
    return (field[None, None], database[None, None])


def solution(mesh):
    in_specs = (
        P("row", "col", None, None),
        P("row", "col", "batch", None),
        P("batch", None),
        P("batch"),
        P("row", "col"),
        P("row", "col", None),
        P("row", "col"),
    )
    out_specs = (P("row", "col", "batch", None), P("row", "col", None, "batch"))
    return jax.shard_map(
        on_device, mesh=mesh, in_specs=in_specs, out_specs=out_specs, check_vma=False
    )
```

```python
import jax
import jax.numpy as jnp
from jax import lax
from jax.sharding import PartitionSpec as P

DB = 128
BLOCKS = 2
SKEW = 1


def passed_along(shard, moment, down, rows, cols):
    pairs = []
    for r in range(rows):
        for c in range(cols):
            if not 0 <= moment - SKEW * (r + c) < BLOCKS:
                continue
            if down and r + 1 < rows:
                pairs.append((r * cols + c, (r + 1) * cols + c))
            if not down and c + 1 < cols:
                pairs.append((r * cols + c, r * cols + c + 1))
    if not pairs:
        return jnp.zeros_like(shard)
    return lax.ppermute(shard, ("row", "col"), pairs)


def on_device(green, background, wavelet, station_cell, fault_point, fault_owner, fault_row):
    row_place = lax.axis_index("row")
    col_place = lax.axis_index("col")
    row_count = lax.axis_size("row")
    col_count = lax.axis_size("col")
    matrix = green[0, 0]
    half = matrix.shape[0] // 2
    to_right, to_lower = lax.optimization_barrier((matrix[:, half:], matrix[:, :half]))
    stations = background.shape[2]
    own_source = (station_cell == row_place * col_count + col_place)[:, None]
    source = background[0, 0].astype(jnp.float32) + jnp.where(
        own_source, wavelet.astype(jnp.float32), 0.0
    )
    height = stations // BLOCKS
    total_fronts = SKEW * (row_count + col_count - 2) + BLOCKS
    down_in = jnp.zeros((height, half), jnp.bfloat16)
    right_in = jnp.zeros((height, half), jnp.bfloat16)
    field = jnp.zeros((stations, 2 * half), jnp.bfloat16)
    inbox = {}
    for moment in range(total_fronts):
        block = moment - SKEW * (row_place + col_place)
        active = jnp.logical_and(block >= 0, block < BLOCKS)
        start = jnp.clip(block, 0, BLOCKS - 1) * height
        part = lax.dynamic_slice_in_dim(source, start, height, 0)
        if moment < SKEW:
            first = background[0, 0, :height].astype(jnp.float32) + jnp.where(
                own_source[:height], wavelet[:height].astype(jnp.float32), 0.0
            )
            lower = first[:, :half].astype(jnp.bfloat16)
            right = first[:, half:].astype(jnp.bfloat16)
        elif moment == SKEW and SKEW == 1:
            down_in, right_in = inbox.pop(moment)
            arrived = down_in + right_in
            rows_from = jnp.where(row_place == 0, half, 0)
            right_rows = lax.dynamic_slice_in_dim(to_right, rows_from, half, 0)
            lower_rows = lax.dynamic_slice_in_dim(to_lower, rows_from, half, 0)
            right = (jnp.dot(arrived, right_rows, preferred_element_type=jnp.float32) + part[:, half:]).astype(jnp.bfloat16)
            lower = (jnp.dot(arrived, lower_rows, preferred_element_type=jnp.float32) + part[:, :half]).astype(jnp.bfloat16)
        else:
            down_in, right_in = inbox.pop(moment)
            joined = jnp.concatenate([down_in, right_in], axis=1)
            right = (jnp.dot(joined, to_right, preferred_element_type=jnp.float32) + part[:, half:]).astype(jnp.bfloat16)
            lower = (jnp.dot(joined, to_lower, preferred_element_type=jnp.float32) + part[:, :half]).astype(jnp.bfloat16)
        right_next = passed_along(right, moment, False, row_count, col_count)
        down_next = passed_along(lower, moment, True, row_count, col_count)
        inbox[moment + SKEW] = (down_next, right_next)
        update = jnp.concatenate([lower, right], axis=1)
        previous = lax.dynamic_slice_in_dim(field, start, height, 0)
        field = lax.dynamic_update_slice_in_dim(field, jnp.where(active, update, previous), start, 0)
    points = fault_point[0]
    owners = fault_owner[0, :, 0]
    targets = fault_row[0]
    listed = points.shape[0]
    point_hot = (points[:, None] == jnp.arange(2 * half, dtype=jnp.int32)[None, :]).astype(jnp.bfloat16)
    traces = jnp.einsum("qp,sp->qs", point_hot, field, preferred_element_type=jnp.float32).astype(jnp.bfloat16)
    capacity = 2 * listed // col_count
    owner_hot = (owners[:, None] == jnp.arange(col_count, dtype=jnp.int32)[None, :]).astype(jnp.int32)
    running = jnp.cumsum(owner_hot, axis=0) - 1
    rank = jnp.sum(owner_hot * running, axis=1)
    slots = owners * capacity + rank
    slot_match = slots[None, :] == jnp.arange(col_count * capacity, dtype=jnp.int32)[:, None]
    slot_hot = slot_match.astype(jnp.bfloat16)
    packed = jnp.dot(slot_hot, traces, preferred_element_type=jnp.float32).astype(jnp.bfloat16)
    slot_rows = jnp.sum(jnp.where(slot_match, targets[None, :] + 1, 0), axis=1) - 1
    tag = jnp.broadcast_to(slot_rows.astype(jnp.bfloat16)[:, None], (col_count * capacity, 128))
    message = jnp.concatenate([packed, tag], axis=1).reshape(col_count, capacity, stations + 128)
    arrived = lax.all_to_all(message, "col", split_axis=0, concat_axis=0, tiled=True)
    arrived = arrived.reshape(col_count * capacity, stations + 128)
    row_numbers = arrived[:, stations].astype(jnp.int32)
    table_hot = (row_numbers[None, :] == jnp.arange(DB, dtype=jnp.int32)[:, None]).astype(jnp.bfloat16)
    database = jnp.dot(table_hot, arrived[:, :stations], preferred_element_type=jnp.float32)
    return (field[None, None], database[None, None])


def solution(mesh):
    in_specs = (
        P("row", "col", None, None),
        P("row", "col", "batch", None),
        P("batch", None),
        P("batch"),
        P("row", "col"),
        P("row", "col", None),
        P("row", "col"),
    )
    out_specs = (P("row", "col", "batch", None), P("row", "col", None, "batch"))
    return jax.shard_map(
        on_device, mesh=mesh, in_specs=in_specs, out_specs=out_specs, check_vma=False
    )
```
